256 devices in a mesh: chan: 64 (over z, x, core), tm: 4 (over y).
Axes of the slice: x: 4, y: 4, z: 8, core: 2. Of those that a mesh axis runs over, the one named last changes fastest.
Arguments:
- voltages: bfloat16 [2, 2, 64, 2048, 2048], P(None, None, None, 'chan', 'tm'), may hold values from -6 to 6
- weights: bfloat16 [64, 2, 2, 32, 2048], P('chan'), may hold values from -0.09375 to 0.09375
- channel_map: int32 [64], replicated, may hold values from 0 to 63, each once
- sweep_response_taps: float32 [64, 2, 32, 256], P('chan', None, 'tm'), may hold values from -6 to 6
- chirp_length: int32 [32], P('tm'), may hold values from 32 to 256, as said below
Outputs:
- dedispersed: float32 [64, 2, 2, 32, 2048], P('chan', None, None, 'tm')
The draws below stay inside these ranges and needn't reach their ends.
Inputs may be any that keep to these rules, and one draw needn't show every extreme that they name: `channel_map`: each channel appears once. `chirp_length`: one beam has the longest chirp of exactly 256 samples.
All inputs are finite; a program needn't handle non-finite values.
Results may differ from the reference program's by a relative error of at most 0.0003.
Values may be sent and summed in bfloat16 or wider, within the bound.
No kernel may reach another device: no remote copies, remote signals or barrier semaphores. Data moves between devices by JAX's collectives and lax.ppermute only.
A program may use at most 128 MiB of HBM per device.

```python
import jax
import jax.numpy as jnp
from jax import lax

ANTENNA_COUNT = 2048
POLARISATION_NUM = 2
BEAM_COUNT = 32
LMAX = 256
CHANNEL_COUNT = 64
TIME_SAMPLES = 2048


def draw_chirp_length(key, part):
    lowest = max(2, LMAX // 8)
    base = jax.random.randint(jax.random.fold_in(key, 11), (BEAM_COUNT,), lowest, LMAX // 2 + 1)
    chosen = jax.random.randint(jax.random.fold_in(key, 12), (), 0, BEAM_COUNT)
    marker = jnp.arange(BEAM_COUNT, dtype=jnp.int32) == chosen
    return jnp.where(marker, LMAX, base).astype(jnp.int32)


def level_of(stream_key, dims, cuts, low, largest):
    factor_of, own = 1.0, jax.random.fold_in(stream_key, 6)
    for axis_at, blocks in cuts:
        draws = jnp.exp(jax.random.uniform(jax.random.fold_in(own, axis_at), (blocks,), jnp.float32, low / len(cuts), largest / len(cuts)))
        factor_of = factor_of * jnp.repeat(draws, dims[axis_at] // blocks).reshape([-1 if axis == axis_at else 1 for axis in range(len(dims))])
    return factor_of


def normal_values(stream_key, shape, spread, limit, pieces=(), kind=jnp.bfloat16):
    values = spread * jax.random.normal(stream_key, shape, jnp.float32)
    if pieces:
        values = values * level_of(stream_key, shape, pieces, -0.22, 0.18)
    return jnp.clip(values, -limit, limit).astype(kind)


def setup_inputs(seed: int = 0) -> dict:
    splits = jax.random.split(jax.random.key(seed), 6)
    voltages = normal_values(splits[0], (2, POLARISATION_NUM, CHANNEL_COUNT, ANTENNA_COUNT, TIME_SAMPLES), 1.0, 6.0, ((3, 64), (4, 4)))
    weights = normal_values(splits[1], (CHANNEL_COUNT, 2, POLARISATION_NUM, BEAM_COUNT, ANTENNA_COUNT), (2 * ANTENNA_COUNT) ** -0.5, 0.09375, ((0, 64),))
    channel_map = jax.random.permutation(splits[2], CHANNEL_COUNT).astype(jnp.int32)
    sweep_response_taps = normal_values(splits[3], (CHANNEL_COUNT, 2, BEAM_COUNT, LMAX), 1.0, 6.0, ((0, 64), (2, 4)), jnp.float32)
    chirp_length = draw_chirp_length(jax.random.fold_in(splits[5], 71), 0)
    return dict(voltages=voltages, weights=weights, channel_map=channel_map, sweep_response_taps=sweep_response_taps, chirp_length=chirp_length)


def reference(voltages, weights, channel_map, sweep_response_taps, chirp_length):
    longest = sweep_response_taps.shape[3]
    total = voltages.shape[4]
    lag = jnp.arange(longest, dtype=jnp.int32)
    inside = lag[None, :] < chirp_length.astype(jnp.int32)[:, None]
    factor = 1.0 / jnp.sqrt(chirp_length.astype(jnp.float32))[:, None]
    high = lax.Precision.HIGHEST

    def one_slot(slot):
        channel = channel_map[slot].astype(jnp.int32)
        volts = lax.dynamic_index_in_dim(voltages, channel, 2, keepdims=False).astype(jnp.float32)
        weight = lax.dynamic_index_in_dim(weights, slot, 0, keepdims=False).astype(jnp.float32)
        taps = lax.dynamic_index_in_dim(sweep_response_taps, slot, 0, keepdims=False)
        beam_real = jnp.einsum('pba,pat->pbt', weight[0], volts[0], precision=high) - jnp.einsum('pba,pat->pbt', weight[1], volts[1], precision=high)
        beam_imag = jnp.einsum('pba,pat->pbt', weight[0], volts[1], precision=high) + jnp.einsum('pba,pat->pbt', weight[1], volts[0], precision=high)
        resp_real = jnp.where(inside, taps[0], 0.0) * factor
        resp_imag = jnp.where(inside, taps[1], 0.0) * factor
        series = beam_real + 1j * beam_imag
        answer = resp_real + 1j * resp_imag
        extent = total + longest
        spectrum = jnp.fft.fft(series, n=extent, axis=-1) * jnp.fft.fft(answer, n=extent, axis=-1)[None]
        result = jnp.fft.ifft(spectrum, axis=-1)[..., :total]
        return jnp.stack([jnp.real(result), jnp.imag(result)], 0).astype(volts.dtype)
    return lax.map(one_slot, jnp.arange(channel_map.shape[0], dtype=jnp.int32))
```

```python
import math

import jax
import jax.numpy as jnp
from jax import lax
from jax.sharding import PartitionSpec as P


def mixing_matrix(weight_rows, axis):
    real_part = lax.index_in_dim(weight_rows, 0, axis, keepdims=False)
    imag_part = lax.index_in_dim(weight_rows, 1, axis, keepdims=False)
    upper = jnp.stack([real_part, -imag_part], axis=-2)
    lower = jnp.stack([imag_part, real_part], axis=-2)
    return jnp.stack([upper, lower], axis=axis)


def fourier_tables(extent):
    counter = jnp.arange(extent, dtype=jnp.int32)
    phase = counter[:, None] * counter[None, :] % extent
    angle = phase.astype(jnp.float32) * (2.0 * math.pi / extent)
    return (jnp.cos(angle), jnp.sin(angle))


def product(left, right):
    return jnp.matmul(left, right, precision=lax.Precision.HIGHEST)


def build_dedispersion(sweep_response_taps, chirp_length):
    longest = sweep_response_taps.shape[3]
    block_size = 2 * longest
    cosines, sines = fourier_tables(block_size)
    lag = jnp.arange(longest, dtype=jnp.int32)
    inside = lag[None, :] < chirp_length[:, None]
    factor = lax.rsqrt(chirp_length.astype(jnp.float32))[:, None]
    resp_real = jnp.where(inside, sweep_response_taps[0, 0], 0.0) * factor
    resp_imag = jnp.where(inside, sweep_response_taps[0, 1], 0.0) * factor
    freq_real = product(resp_real, cosines[:longest]) + product(resp_imag, sines[:longest])
    freq_imag = product(resp_imag, cosines[:longest]) - product(resp_real, sines[:longest])
    gain_real = freq_real[:, None, :]
    gain_imag = freq_imag[:, None, :]
    back_cos = cosines[:, longest:]
    back_sin = sines[:, longest:]

    def dedisperse(series):
        total = series.shape[3]
        count = total // longest
        padding = jnp.zeros(series.shape[:3] + (longest,), jnp.float32)
        padded = jnp.concatenate([padding, series], axis=3)
        front = padded[..., :total].reshape(series.shape[:3] + (count, longest))
        behind = padded[..., longest:].reshape(series.shape[:3] + (count, longest))
        blocks = jnp.concatenate([front, behind], axis=4)
        spec_real = product(blocks[0], cosines) + product(blocks[1], sines)
        spec_imag = product(blocks[1], cosines) - product(blocks[0], sines)
        prod_real = spec_real * gain_real - spec_imag * gain_imag
        prod_imag = spec_real * gain_imag + spec_imag * gain_real
        out_real = (product(prod_real, back_cos) - product(prod_imag, back_sin)) / block_size
        out_imag = (product(prod_imag, back_cos) + product(prod_real, back_sin)) / block_size
        return jnp.stack([out_real, out_imag], 0).reshape(series.shape)

    return dedisperse


def on_device(voltages, weights, channel_map, sweep_response_taps, chirp_length):
    selected = jnp.take(voltages, channel_map, axis=2)
    local_weights = lax.all_to_all(weights, "chan", split_axis=4, concat_axis=0, tiled=True)
    mixing = mixing_matrix(local_weights, 1)
    partial = jnp.einsum(
        "jopbra,rpjat->jopbt",
        mixing,
        selected,
        preferred_element_type=jnp.float32,
    )
    beams = lax.psum_scatter(partial, "chan", scatter_dimension=0, tiled=True)[0]
    dedisperse = build_dedispersion(sweep_response_taps, chirp_length)
    result = dedisperse(lax.all_to_all(beams, "tm", split_axis=2, concat_axis=3, tiled=True))
    return result[None]


def solution(mesh):
    return jax.shard_map(
        on_device,
        mesh=mesh,
        in_specs=(
            P(None, None, None, "chan", "tm"),
            P("chan", None, None, None, None),
            P(),
            P("chan", None, "tm", None),
            P("tm"),
        ),
        out_specs=P("chan", None, None, "tm", None),
        check_vma=False,
    )
```

```python
import math

import jax
import jax.numpy as jnp
from jax import lax
from jax.sharding import PartitionSpec as P


def mixing_matrix(weight_rows, axis):
    real_part = lax.index_in_dim(weight_rows, 0, axis, keepdims=False)
    imag_part = lax.index_in_dim(weight_rows, 1, axis, keepdims=False)
    upper = jnp.stack([real_part, -imag_part], axis=-2)
    lower = jnp.stack([imag_part, real_part], axis=-2)
    return jnp.stack([upper, lower], axis=axis)


def fourier_tables(extent):
    counter = jnp.arange(extent, dtype=jnp.int32)
    phase = counter[:, None] * counter[None, :] % extent
    angle = phase.astype(jnp.float32) * (2.0 * math.pi / extent)
    return (jnp.cos(angle), jnp.sin(angle))


def product(left, right):
    return jnp.matmul(left, right, precision=lax.Precision.HIGHEST)


def build_dedispersion(sweep_response_taps, chirp_length):
    longest = sweep_response_taps.shape[3]
    block_size = 2 * longest
    cosines, sines = fourier_tables(block_size)
    lag = jnp.arange(longest, dtype=jnp.int32)
    inside = lag[None, :] < chirp_length[:, None]
    factor = lax.rsqrt(chirp_length.astype(jnp.float32))[:, None]
    resp_real = jnp.where(inside, sweep_response_taps[0, 0], 0.0) * factor
    resp_imag = jnp.where(inside, sweep_response_taps[0, 1], 0.0) * factor
    freq_real = product(resp_real, cosines[:longest]) + product(resp_imag, sines[:longest])
    freq_imag = product(resp_imag, cosines[:longest]) - product(resp_real, sines[:longest])
    gain_real = freq_real[:, None, :]
    gain_imag = freq_imag[:, None, :]
    back_cos = cosines[:, longest:]
    back_sin = sines[:, longest:]

    def dedisperse(series):
        total = series.shape[3]
        count = total // longest
        padding = jnp.zeros(series.shape[:3] + (longest,), jnp.float32)
        padded = jnp.concatenate([padding, series], axis=3)
        front = padded[..., :total].reshape(series.shape[:3] + (count, longest))
        behind = padded[..., longest:].reshape(series.shape[:3] + (count, longest))
        blocks = jnp.concatenate([front, behind], axis=4)
        spec_real = product(blocks[0], cosines) + product(blocks[1], sines)
        spec_imag = product(blocks[1], cosines) - product(blocks[0], sines)
        prod_real = spec_real * gain_real - spec_imag * gain_imag
        prod_imag = spec_real * gain_imag + spec_imag * gain_real
        out_real = (product(prod_real, back_cos) - product(prod_imag, back_sin)) / block_size
        out_imag = (product(prod_imag, back_cos) + product(prod_real, back_sin)) / block_size
        return jnp.stack([out_real, out_imag], 0).reshape(series.shape)

    return dedisperse


def ring_reduce_scatter(chunks, axis, size, chunk_axis, split_axis):
    position = lax.axis_index(axis)
    halves = jnp.split(chunks, 2, axis=split_axis)
    forward = [(i, (i + 1) % size) for i in range(size)]
    backward = [(i, (i - 1) % size) for i in range(size)]

    def pick(part, index):
        return lax.dynamic_index_in_dim(part, index % size, chunk_axis, keepdims=False)

    acc_cw = pick(halves[0], position - 1)
    acc_ccw = pick(halves[1], position + 1)
    for step in range(size - 1):
        acc_cw = lax.ppermute(acc_cw, axis, forward) + pick(halves[0], position - step - 2)
        acc_ccw = lax.ppermute(acc_ccw, axis, backward) + pick(halves[1], position + step + 2)
    return jnp.concatenate([acc_cw, acc_ccw], axis=split_axis - 1)


def on_device(voltages, weights, channel_map, sweep_response_taps, chirp_length):
    zs, xs, cs = lax.axis_size("z"), lax.axis_size("x"), lax.axis_size("c")
    selected = jnp.take(voltages, channel_map, axis=2)
    r, p, slots, ants, times = selected.shape
    selected = selected.reshape(r, p, zs, xs, cs, ants, times)
    own = lax.all_to_all(selected, "c", split_axis=4, concat_axis=5, tiled=True)[:, :, :, :, 0]
    local_weights = lax.all_to_all(weights, ("z", "x"), split_axis=4, concat_axis=0, tiled=True)
    local_weights = local_weights.reshape((zs, xs) + local_weights.shape[1:])
    mixing = mixing_matrix(local_weights, 2)
    partial = jnp.einsum(
        "zxopbra,rpzxat->xzopbt",
        mixing,
        own,
        preferred_element_type=jnp.float32,
    )
    partial = ring_reduce_scatter(partial, "x", xs, 0, 2)
    beams = ring_reduce_scatter(partial, "z", zs, 0, 1)
    dedisperse = build_dedispersion(sweep_response_taps, chirp_length)
    result = dedisperse(lax.all_to_all(beams, "tm", split_axis=2, concat_axis=3, tiled=True))
    return result[None]


def solution(mesh):
    chan = mesh.shape["chan"]
    zs = 8 if chan % 8 == 0 and chan >= 16 else 1
    grid = mesh.devices.reshape(zs, chan // zs // 2, 2, mesh.shape["tm"])
    fine = jax.sharding.Mesh(grid, ("z", "x", "c", "tm"))
    antennas = ("z", "x", "c")
    return jax.shard_map(
        on_device,
        mesh=fine,
        in_specs=(
            P(None, None, None, antennas, "tm"),
            P(antennas, None, None, None, None),
            P(),
            P(antennas, None, "tm", None),
            P("tm"),
        ),
        out_specs=P(antennas, None, None, "tm", None),
        check_vma=False,
    )
```

```python
import math

import jax
import jax.numpy as jnp
from jax import lax
from jax.sharding import PartitionSpec as P


def mixing_matrix(weight_rows, axis):
    real_part = lax.index_in_dim(weight_rows, 0, axis, keepdims=False)
    imag_part = lax.index_in_dim(weight_rows, 1, axis, keepdims=False)
    upper = jnp.stack([real_part, -imag_part], axis=-2)
    lower = jnp.stack([imag_part, real_part], axis=-2)
    return jnp.stack([upper, lower], axis=axis)


def fourier_tables(extent):
    counter = jnp.arange(extent, dtype=jnp.int32)
    phase = counter[:, None] * counter[None, :] % extent
    angle = phase.astype(jnp.float32) * (2.0 * math.pi / extent)
    return (jnp.cos(angle), jnp.sin(angle))


def product(left, right):
    return jnp.matmul(left, right, precision=lax.Precision.HIGHEST)


def build_dedispersion(sweep_response_taps, chirp_length):
    longest = sweep_response_taps.shape[3]
    block_size = 2 * longest
    cosines, sines = fourier_tables(block_size)
    lag = jnp.arange(longest, dtype=jnp.int32)
    inside = lag[None, :] < chirp_length[:, None]
    factor = lax.rsqrt(chirp_length.astype(jnp.float32))[:, None]
    resp_real = jnp.where(inside, sweep_response_taps[0, 0], 0.0) * factor
    resp_imag = jnp.where(inside, sweep_response_taps[0, 1], 0.0) * factor
    freq_real = product(resp_real, cosines[:longest]) + product(resp_imag, sines[:longest])
    freq_imag = product(resp_imag, cosines[:longest]) - product(resp_real, sines[:longest])
    gain_real = freq_real[:, None, :]
    gain_imag = freq_imag[:, None, :]
    back_cos = cosines[:, longest:]
    back_sin = sines[:, longest:]

    def dedisperse(series):
        total = series.shape[3]
        count = total // longest
        padding = jnp.zeros(series.shape[:3] + (longest,), jnp.float32)
        padded = jnp.concatenate([padding, series], axis=3)
        front = padded[..., :total].reshape(series.shape[:3] + (count, longest))
        behind = padded[..., longest:].reshape(series.shape[:3] + (count, longest))
        blocks = jnp.concatenate([front, behind], axis=4)
        spec_real = product(blocks[0], cosines) + product(blocks[1], sines)
        spec_imag = product(blocks[1], cosines) - product(blocks[0], sines)
        prod_real = spec_real * gain_real - spec_imag * gain_imag
        prod_imag = spec_real * gain_imag + spec_imag * gain_real
        out_real = (product(prod_real, back_cos) - product(prod_imag, back_sin)) / block_size
        out_imag = (product(prod_imag, back_cos) + product(prod_real, back_sin)) / block_size
        return jnp.stack([out_real, out_imag], 0).reshape(series.shape)

    return dedisperse


def ring_reduce_scatter(chunks, axis, size, split_axis):
    position = lax.axis_index(axis)
    halves = jnp.split(chunks, 2, axis=split_axis)
    forward = [(i, (i + 1) % size) for i in range(size)]
    backward = [(i, (i - 1) % size) for i in range(size)]

    def pick(part, index):
        return lax.dynamic_index_in_dim(part, index % size, 0, keepdims=False)

    acc_cw = pick(halves[0], position - 1)
    acc_ccw = pick(halves[1], position + 1)
    for step in range(size - 1):
        acc_cw = lax.ppermute(acc_cw, axis, forward) + pick(halves[0], position - step - 2)
        acc_ccw = lax.ppermute(acc_ccw, axis, backward) + pick(halves[1], position + step + 2)
    return jnp.concatenate([acc_cw, acc_ccw], axis=split_axis - 1)


def on_device(voltages, weights, channel_map, sweep_response_taps, chirp_length):
    zs, xs, cs = lax.axis_size("z"), lax.axis_size("x"), lax.axis_size("c")
    order = channel_map.reshape(zs, xs, cs).transpose(2, 0, 1)
    selected = jnp.moveaxis(jnp.take(voltages, order, axis=2, mode="clip"), 2, 0)
    own = lax.all_to_all(selected, "c", split_axis=0, concat_axis=5, tiled=True)[0]
    local_weights = lax.all_to_all(weights, ("z", "x"), split_axis=4, concat_axis=0, tiled=True)
    local_weights = local_weights.reshape((zs, xs) + local_weights.shape[1:])
    mixing = mixing_matrix(local_weights, 2)
    partial = jnp.einsum(
        "zxopbra,rpzxat->zxopbt",
        mixing,
        own,
        preferred_element_type=jnp.float32,
    )
    partial = ring_reduce_scatter(partial, "z", zs, 2)
    beams = ring_reduce_scatter(partial, "x", xs, 1)
    dedisperse = build_dedispersion(sweep_response_taps, chirp_length)
    result = dedisperse(lax.all_to_all(beams, "tm", split_axis=2, concat_axis=3, tiled=True))
    return result[None]


def solution(mesh):
    chan = mesh.shape["chan"]
    zs = 8 if chan % 8 == 0 and chan >= 16 else 1
    grid = mesh.devices.reshape(zs, chan // zs // 2, 2, mesh.shape["tm"])
    fine = jax.sharding.Mesh(grid, ("z", "x", "c", "tm"))
    antennas = ("z", "x", "c")
    return jax.shard_map(
        on_device,
        mesh=fine,
        in_specs=(
            P(None, None, None, antennas, "tm"),
            P(antennas, None, None, None, None),
            P(),
            P(antennas, None, "tm", None),
            P("tm"),
        ),
        out_specs=P(antennas, None, None, "tm", None),
        check_vma=False,
    )
```

```python
import math

import jax
import jax.numpy as jnp
from jax import lax
from jax.sharding import PartitionSpec as P


def mixing_matrix(weight_rows, axis):
    real_part = lax.index_in_dim(weight_rows, 0, axis, keepdims=False)
    imag_part = lax.index_in_dim(weight_rows, 1, axis, keepdims=False)
    upper = jnp.stack([real_part, -imag_part], axis=-2)
    lower = jnp.stack([imag_part, real_part], axis=-2)
    return jnp.stack([upper, lower], axis=axis)


def fourier_tables(extent):
    counter = jnp.arange(extent, dtype=jnp.int32)
    phase = counter[:, None] * counter[None, :] % extent
    angle = phase.astype(jnp.float32) * (2.0 * math.pi / extent)
    return (jnp.cos(angle), jnp.sin(angle))


def product(left, right):
    return jnp.matmul(left, right, precision=lax.Precision.HIGHEST)


def build_dedispersion(sweep_response_taps, chirp_length):
    longest = sweep_response_taps.shape[3]
    block_size = 2 * longest
    cosines, sines = fourier_tables(block_size)
    lag = jnp.arange(longest, dtype=jnp.int32)
    inside = lag[None, :] < chirp_length[:, None]
    factor = lax.rsqrt(chirp_length.astype(jnp.float32))[:, None]
    resp_real = jnp.where(inside, sweep_response_taps[0, 0], 0.0) * factor
    resp_imag = jnp.where(inside, sweep_response_taps[0, 1], 0.0) * factor
    freq_real = product(resp_real, cosines[:longest]) + product(resp_imag, sines[:longest])
    freq_imag = product(resp_imag, cosines[:longest]) - product(resp_real, sines[:longest])
    gain_real = freq_real[:, None, :]
    gain_imag = freq_imag[:, None, :]
    back_cos = cosines[:, longest:]
    back_sin = sines[:, longest:]

    def dedisperse(series):
        total = series.shape[3]
        count = total // longest
        padding = jnp.zeros(series.shape[:3] + (longest,), jnp.float32)
        padded = jnp.concatenate([padding, series], axis=3)
        front = padded[..., :total].reshape(series.shape[:3] + (count, longest))
        behind = padded[..., longest:].reshape(series.shape[:3] + (count, longest))
        blocks = jnp.concatenate([front, behind], axis=4)
        spec_real = product(blocks[0], cosines) + product(blocks[1], sines)
        spec_imag = product(blocks[1], cosines) - product(blocks[0], sines)
        prod_real = spec_real * gain_real - spec_imag * gain_imag
        prod_imag = spec_real * gain_imag + spec_imag * gain_real
        out_real = (product(prod_real, back_cos) - product(prod_imag, back_sin)) / block_size
        out_imag = (product(prod_imag, back_cos) + product(prod_real, back_sin)) / block_size
        return jnp.stack([out_real, out_imag], 0).reshape(series.shape)

    return dedisperse


def ring_reduce_scatter(chunks, axis, size, split_axis):
    position = lax.axis_index(axis)
    halves = jnp.split(chunks, 2, axis=split_axis)
    forward = [(i, (i + 1) % size) for i in range(size)]
    backward = [(i, (i - 1) % size) for i in range(size)]

    def pick(part, index):
        return lax.dynamic_index_in_dim(part, index % size, 0, keepdims=False)

    acc_cw = pick(halves[0], position - 1)
    acc_ccw = pick(halves[1], position + 1)
    for step in range(size - 1):
        acc_cw = lax.ppermute(acc_cw, axis, forward) + pick(halves[0], position - step - 2)
        acc_ccw = lax.ppermute(acc_ccw, axis, backward) + pick(halves[1], position + step + 2)
    return jnp.concatenate([acc_cw, acc_ccw], axis=split_axis - 1)


def on_device(voltages, weights, channel_map, sweep_response_taps, chirp_length):
    zs, xs, cs = lax.axis_size("z"), lax.axis_size("x"), lax.axis_size("c")
    order = channel_map.reshape(zs, xs, cs).transpose(2, 0, 1)
    selected = jnp.moveaxis(jnp.take(voltages, order, axis=2, mode="clip"), 2, 0)
    own = lax.all_to_all(selected, "c", split_axis=0, concat_axis=5, tiled=True)[0]
    local_weights = lax.all_to_all(weights, ("z", "x"), split_axis=4, concat_axis=0, tiled=True)
    local_weights = local_weights.reshape((zs, xs) + local_weights.shape[1:])
    mixing = mixing_matrix(local_weights, 2)
    real_part = jnp.einsum(
        "zxpbra,rpzxat->zxpbt", mixing[:, :, 0], own, preferred_element_type=jnp.float32
    )
    imag_part = jnp.einsum(
        "zxpbra,rpzxat->xzpbt", mixing[:, :, 1], own, preferred_element_type=jnp.float32
    )
    real_part = ring_reduce_scatter(ring_reduce_scatter(real_part, "z", zs, 2), "x", xs, 1)
    imag_part = ring_reduce_scatter(imag_part, "x", xs, 2)
    imag_part = lax.psum_scatter(imag_part, "z", scatter_dimension=0, tiled=True)[0]
    beams = jnp.stack([real_part, imag_part], axis=0)
    dedisperse = build_dedispersion(sweep_response_taps, chirp_length)
    result = dedisperse(lax.all_to_all(beams, "tm", split_axis=2, concat_axis=3, tiled=True))
    return result[None]


def solution(mesh):
    chan = mesh.shape["chan"]
    zs = 8 if chan % 8 == 0 and chan >= 16 else 1
    grid = mesh.devices.reshape(zs, chan // zs // 2, 2, mesh.shape["tm"])
    fine = jax.sharding.Mesh(grid, ("z", "x", "c", "tm"))
    antennas = ("z", "x", "c")
    return jax.shard_map(
        on_device,
        mesh=fine,
        in_specs=(
            P(None, None, None, antennas, "tm"),
            P(antennas, None, None, None, None),
            P(),
            P(antennas, None, "tm", None),
            P("tm"),
        ),
        out_specs=P(antennas, None, None, "tm", None),
        check_vma=False,
    )
```

```python
import math

import jax
import jax.numpy as jnp
from jax import lax
from jax.experimental import pallas as pl
from jax.experimental.pallas import tpu as pltpu
from jax.sharding import PartitionSpec as P


def mixing_matrix(weight_rows, axis):
    real_part = lax.index_in_dim(weight_rows, 0, axis, keepdims=False)
    imag_part = lax.index_in_dim(weight_rows, 1, axis, keepdims=False)
    upper = jnp.stack([real_part, -imag_part], axis=-2)
    lower = jnp.stack([imag_part, real_part], axis=-2)
    return jnp.stack([upper, lower], axis=axis)


def fourier_tables(extent):
    counter = jnp.arange(extent, dtype=jnp.int32)
    phase = counter[:, None] * counter[None, :] % extent
    angle = phase.astype(jnp.float32) * (2.0 * math.pi / extent)
    return (jnp.cos(angle), jnp.sin(angle))


def product(left, right):
    return jnp.matmul(left, right, precision=lax.Precision.HIGHEST)


def build_dedispersion(sweep_response_taps, chirp_length):
    longest = sweep_response_taps.shape[3]
    block_size = 2 * longest
    cosines, sines = fourier_tables(block_size)
    lag = jnp.arange(longest, dtype=jnp.int32)
    inside = lag[None, :] < chirp_length[:, None]
    factor = lax.rsqrt(chirp_length.astype(jnp.float32))[:, None]
    resp_real = jnp.where(inside, sweep_response_taps[0, 0], 0.0) * factor
    resp_imag = jnp.where(inside, sweep_response_taps[0, 1], 0.0) * factor
    freq_real = product(resp_real, cosines[:longest]) + product(resp_imag, sines[:longest])
    freq_imag = product(resp_imag, cosines[:longest]) - product(resp_real, sines[:longest])
    gain_real = freq_real[:, None, :]
    gain_imag = freq_imag[:, None, :]
    back_cos = cosines[:, longest:]
    back_sin = sines[:, longest:]

    def dedisperse(series):
        total = series.shape[3]
        count = total // longest
        padding = jnp.zeros(series.shape[:3] + (longest,), jnp.float32)
        padded = jnp.concatenate([padding, series], axis=3)
        front = padded[..., :total].reshape(series.shape[:3] + (count, longest))
        behind = padded[..., longest:].reshape(series.shape[:3] + (count, longest))
        blocks = jnp.concatenate([front, behind], axis=4)
        spec_real = product(blocks[0], cosines) + product(blocks[1], sines)
        spec_imag = product(blocks[1], cosines) - product(blocks[0], sines)
        prod_real = spec_real * gain_real - spec_imag * gain_imag
        prod_imag = spec_real * gain_imag + spec_imag * gain_real
        out_real = (product(prod_real, back_cos) - product(prod_imag, back_sin)) / block_size
        out_imag = (product(prod_imag, back_cos) + product(prod_real, back_sin)) / block_size
        return jnp.stack([out_real, out_imag], 0).reshape(series.shape)

    return dedisperse


def ring_reduce_scatter(chunks, axis, size, split_axis):
    position = lax.axis_index(axis)
    halves = jnp.split(chunks, 2, axis=split_axis)
    forward = [(i, (i + 1) % size) for i in range(size)]
    backward = [(i, (i - 1) % size) for i in range(size)]

    def pick(part, index):
        return lax.dynamic_index_in_dim(part, index % size, 0, keepdims=False)

    acc_cw = pick(halves[0], position - 1)
    acc_ccw = pick(halves[1], position + 1)
    for step in range(size - 1):
        acc_cw = lax.ppermute(acc_cw, axis, forward) + pick(halves[0], position - step - 2)
        acc_ccw = lax.ppermute(acc_ccw, axis, backward) + pick(halves[1], position + step + 2)
    return jnp.concatenate([acc_cw, acc_ccw], axis=split_axis - 1)


def select_channels(voltages, channel_map, zs, xs, cs):
    r, p, slots, ants, times = voltages.shape

    def kernel(map_ref, v_hbm, o_hbm, sems):
        copies = []
        for z in range(zs):
            for x in range(xs):
                for c in range(cs):
                    slot = (z * xs + x) * cs + c
                    copy = pltpu.make_async_copy(
                        v_hbm.at[:, :, map_ref[slot]], o_hbm.at[c, :, :, z, x], sems.at[slot]
                    )
                    copy.start()
                    copies.append(copy)
        for copy in copies:
            copy.wait()

    return pl.pallas_call(
        kernel,
        out_shape=jax.ShapeDtypeStruct((cs, r, p, zs, xs, ants, times), voltages.dtype),
        in_specs=[
            pl.BlockSpec(memory_space=pltpu.SMEM),
            pl.BlockSpec(memory_space=pl.ANY),
        ],
        out_specs=pl.BlockSpec(memory_space=pl.ANY),
        scratch_shapes=[pltpu.SemaphoreType.DMA((slots,))],
    )(channel_map, voltages)


def on_device(voltages, weights, channel_map, sweep_response_taps, chirp_length):
    zs, xs, cs = lax.axis_size("z"), lax.axis_size("x"), lax.axis_size("c")
    selected = select_channels(voltages, channel_map, zs, xs, cs)
    own = lax.all_to_all(selected, "c", split_axis=0, concat_axis=0, tiled=True)
    local_weights = lax.all_to_all(weights, ("z", "x"), split_axis=4, concat_axis=0, tiled=True)
    local_weights = local_weights.reshape((zs, xs) + local_weights.shape[1:4] + (cs, -1))
    mixing = mixing_matrix(local_weights, 2)
    partial = jnp.einsum(
        "zxopbcra,crpzxat->zxopbt",
        mixing,
        own,
        preferred_element_type=jnp.float32,
    )
    partial = ring_reduce_scatter(partial, "z", zs, 2)
    beams = ring_reduce_scatter(partial, "x", xs, 1)
    dedisperse = build_dedispersion(sweep_response_taps, chirp_length)
    result = dedisperse(lax.all_to_all(beams, "tm", split_axis=2, concat_axis=3, tiled=True))
    return result[None]


def solution(mesh):
    chan = mesh.shape["chan"]
    zs = 8 if chan % 8 == 0 and chan >= 16 else 1
    grid = mesh.devices.reshape(zs, chan // zs // 2, 2, mesh.shape["tm"])
    fine = jax.sharding.Mesh(grid, ("z", "x", "c", "tm"))
    antennas = ("z", "x", "c")
    return jax.shard_map(
        on_device,
        mesh=fine,
        in_specs=(
            P(None, None, None, antennas, "tm"),
            P(antennas, None, None, None, None),
            P(),
            P(antennas, None, "tm", None),
            P("tm"),
        ),
        out_specs=P(antennas, None, None, "tm", None),
        check_vma=False,
    )
```

```python
import math

import jax
import jax.numpy as jnp
from jax import lax
from jax.sharding import PartitionSpec as P


def mixing_matrix(weight_rows, axis):
    real_part = lax.index_in_dim(weight_rows, 0, axis, keepdims=False)
    imag_part = lax.index_in_dim(weight_rows, 1, axis, keepdims=False)
    upper = jnp.stack([real_part, -imag_part], axis=-2)
    lower = jnp.stack([imag_part, real_part], axis=-2)
    return jnp.stack([upper, lower], axis=axis)


def fourier_tables(extent):
    counter = jnp.arange(extent, dtype=jnp.int32)
    phase = counter[:, None] * counter[None, :] % extent
    angle = phase.astype(jnp.float32) * (2.0 * math.pi / extent)
    return (jnp.cos(angle), jnp.sin(angle))


def product(left, right):
    return jnp.matmul(left, right, precision=lax.Precision.HIGHEST)


def build_dedispersion(sweep_response_taps, chirp_length):
    longest = sweep_response_taps.shape[3]
    block_size = 2 * longest
    cosines, sines = fourier_tables(block_size)
    lag = jnp.arange(longest, dtype=jnp.int32)
    inside = lag[None, :] < chirp_length[:, None]
    factor = lax.rsqrt(chirp_length.astype(jnp.float32))[:, None]
    resp_real = jnp.where(inside, sweep_response_taps[0, 0], 0.0) * factor
    resp_imag = jnp.where(inside, sweep_response_taps[0, 1], 0.0) * factor
    freq_real = product(resp_real, cosines[:longest]) + product(resp_imag, sines[:longest])
    freq_imag = product(resp_imag, cosines[:longest]) - product(resp_real, sines[:longest])
    gain_real = freq_real[:, None, :]
    gain_imag = freq_imag[:, None, :]
    back_cos = cosines[:, longest:]
    back_sin = sines[:, longest:]

    def dedisperse(series):
        total = series.shape[3]
        count = total // longest
        padding = jnp.zeros(series.shape[:3] + (longest,), jnp.float32)
        padded = jnp.concatenate([padding, series], axis=3)
        front = padded[..., :total].reshape(series.shape[:3] + (count, longest))
        behind = padded[..., longest:].reshape(series.shape[:3] + (count, longest))
        blocks = jnp.concatenate([front, behind], axis=4)
        spec_real = product(blocks[0], cosines) + product(blocks[1], sines)
        spec_imag = product(blocks[1], cosines) - product(blocks[0], sines)
        prod_real = spec_real * gain_real - spec_imag * gain_imag
        prod_imag = spec_real * gain_imag + spec_imag * gain_real
        out_real = (product(prod_real, back_cos) - product(prod_imag, back_sin)) / block_size
        out_imag = (product(prod_imag, back_cos) + product(prod_real, back_sin)) / block_size
        return jnp.stack([out_real, out_imag], 0).reshape(series.shape)

    return dedisperse


def ring_reduce_scatter(chunks, axis, size, split_axis):
    position = lax.axis_index(axis)
    halves = jnp.split(chunks, 2, axis=split_axis)
    forward = [(i, (i + 1) % size) for i in range(size)]
    backward = [(i, (i - 1) % size) for i in range(size)]

    def pick(part, index):
        return lax.dynamic_index_in_dim(part, index % size, 0, keepdims=False)

    acc_cw = pick(halves[0], position - 1)
    acc_ccw = pick(halves[1], position + 1)
    for step in range(size - 1):
        acc_cw = lax.ppermute(acc_cw, axis, forward) + pick(halves[0], position - step - 2)
        acc_ccw = lax.ppermute(acc_ccw, axis, backward) + pick(halves[1], position + step + 2)
    return jnp.concatenate([acc_cw, acc_ccw], axis=split_axis - 1)


def on_device(voltages, weights, channel_map, sweep_response_taps, chirp_length):
    zs, xs, cs = lax.axis_size("z"), lax.axis_size("x"), lax.axis_size("c")
    order = channel_map.reshape(zs, xs, cs).transpose(2, 0, 1)
    selected = jnp.moveaxis(jnp.take(voltages, order, axis=2, mode="clip"), 2, 0)
    local_weights = lax.all_to_all(weights, ("z", "x"), split_axis=4, concat_axis=0, tiled=True)
    selected, local_weights = lax.optimization_barrier((selected, local_weights))
    own = lax.all_to_all(selected, "c", split_axis=0, concat_axis=5, tiled=True)[0]
    local_weights = local_weights.reshape((zs, xs) + local_weights.shape[1:])
    mixing = mixing_matrix(local_weights, 2)
    partial = jnp.einsum(
        "zxopbra,rpzxat->zxopbt",
        mixing,
        own,
        preferred_element_type=jnp.float32,
    )
    partial = ring_reduce_scatter(partial, "z", zs, 2)
    beams = ring_reduce_scatter(partial, "x", xs, 1)
    dedisperse = build_dedispersion(sweep_response_taps, chirp_length)
    result = dedisperse(lax.all_to_all(beams, "tm", split_axis=2, concat_axis=3, tiled=True))
    return result[None]


def solution(mesh):
    chan = mesh.shape["chan"]
    zs = 8 if chan % 8 == 0 and chan >= 16 else 1
    grid = mesh.devices.reshape(zs, chan // zs // 2, 2, mesh.shape["tm"])
    fine = jax.sharding.Mesh(grid, ("z", "x", "c", "tm"))
    antennas = ("z", "x", "c")
    return jax.shard_map(
        on_device,
        mesh=fine,
        in_specs=(
            P(None, None, None, antennas, "tm"),
            P(antennas, None, None, None, None),
            P(),
            P(antennas, None, "tm", None),
            P("tm"),
        ),
        out_specs=P(antennas, None, None, "tm", None),
        check_vma=False,
    )
```

```python
import math

import jax
import jax.numpy as jnp
from jax import lax
from jax.sharding import PartitionSpec as P


def mixing_matrix(weight_rows, axis):
    real_part = lax.index_in_dim(weight_rows, 0, axis, keepdims=False)
    imag_part = lax.index_in_dim(weight_rows, 1, axis, keepdims=False)
    upper = jnp.stack([real_part, -imag_part], axis=-2)
    lower = jnp.stack([imag_part, real_part], axis=-2)
    return jnp.stack([upper, lower], axis=axis)


def fourier_tables(extent):
    counter = jnp.arange(extent, dtype=jnp.int32)
    phase = counter[:, None] * counter[None, :] % extent
    angle = phase.astype(jnp.float32) * (2.0 * math.pi / extent)
    return (jnp.cos(angle), jnp.sin(angle))


def product(left, right):
    return jnp.matmul(left, right, precision=lax.Precision.HIGH)


def build_dedispersion(sweep_response_taps, chirp_length):
    longest = sweep_response_taps.shape[3]
    block_size = 2 * longest
    cosines, sines = fourier_tables(block_size)
    lag = jnp.arange(longest, dtype=jnp.int32)
    inside = lag[None, :] < chirp_length[:, None]
    factor = lax.rsqrt(chirp_length.astype(jnp.float32))[:, None]
    resp_real = jnp.where(inside, sweep_response_taps[0, 0], 0.0) * factor
    resp_imag = jnp.where(inside, sweep_response_taps[0, 1], 0.0) * factor
    freq_real = product(resp_real, cosines[:longest]) + product(resp_imag, sines[:longest])
    freq_imag = product(resp_imag, cosines[:longest]) - product(resp_real, sines[:longest])
    gain_real = freq_real[:, None, :]
    gain_imag = freq_imag[:, None, :]
    back_cos = cosines[:, longest:]
    back_sin = sines[:, longest:]

    def dedisperse(series):
        total = series.shape[3]
        count = total // longest
        padding = jnp.zeros(series.shape[:3] + (longest,), jnp.float32)
        padded = jnp.concatenate([padding, series], axis=3)
        front = padded[..., :total].reshape(series.shape[:3] + (count, longest))
        behind = padded[..., longest:].reshape(series.shape[:3] + (count, longest))
        blocks = jnp.concatenate([front, behind], axis=4)
        spec_real = product(blocks[0], cosines) + product(blocks[1], sines)
        spec_imag = product(blocks[1], cosines) - product(blocks[0], sines)
        prod_real = spec_real * gain_real - spec_imag * gain_imag
        prod_imag = spec_real * gain_imag + spec_imag * gain_real
        out_real = (product(prod_real, back_cos) - product(prod_imag, back_sin)) / block_size
        out_imag = (product(prod_imag, back_cos) + product(prod_real, back_sin)) / block_size
        return jnp.stack([out_real, out_imag], 0).reshape(series.shape)

    return dedisperse


def ring_reduce_scatter(chunks, axis, size, split_axis):
    position = lax.axis_index(axis)
    halves = jnp.split(chunks, 2, axis=split_axis)
    forward = [(i, (i + 1) % size) for i in range(size)]
    backward = [(i, (i - 1) % size) for i in range(size)]

    def pick(part, index):
        return lax.dynamic_index_in_dim(part, index % size, 0, keepdims=False)

    acc_cw = pick(halves[0], position - 1)
    acc_ccw = pick(halves[1], position + 1)
    for step in range(size - 1):
        acc_cw = lax.ppermute(acc_cw, axis, forward) + pick(halves[0], position - step - 2)
        acc_ccw = lax.ppermute(acc_ccw, axis, backward) + pick(halves[1], position + step + 2)
    return jnp.concatenate([acc_cw, acc_ccw], axis=split_axis - 1)


def on_device(voltages, weights, channel_map, sweep_response_taps, chirp_length):
    zs, xs, cs = lax.axis_size("z"), lax.axis_size("x"), lax.axis_size("c")
    order = channel_map.reshape(zs, xs, cs).transpose(2, 0, 1)
    selected = jnp.moveaxis(jnp.take(voltages, order, axis=2, mode="clip"), 2, 0)
    own = lax.all_to_all(selected, "c", split_axis=0, concat_axis=5, tiled=True)[0]
    local_weights = lax.all_to_all(weights, ("z", "x"), split_axis=4, concat_axis=0, tiled=True)
    local_weights = local_weights.reshape((zs, xs) + local_weights.shape[1:])
    mixing = mixing_matrix(local_weights, 2)
    partial = jnp.einsum(
        "zxopbra,rpzxat->zxopbt",
        mixing,
        own,
        preferred_element_type=jnp.float32,
    )
    partial = ring_reduce_scatter(partial, "z", zs, 2)
    beams = ring_reduce_scatter(partial, "x", xs, 1)
    dedisperse = build_dedispersion(sweep_response_taps, chirp_length)
    result = dedisperse(lax.all_to_all(beams, "tm", split_axis=2, concat_axis=3, tiled=True))
    return result[None]


def solution(mesh):
    chan = mesh.shape["chan"]
    zs = 8 if chan % 8 == 0 and chan >= 16 else 1
    grid = mesh.devices.reshape(zs, chan // zs // 2, 2, mesh.shape["tm"])
    fine = jax.sharding.Mesh(grid, ("z", "x", "c", "tm"))
    antennas = ("z", "x", "c")
    return jax.shard_map(
        on_device,
        mesh=fine,
        in_specs=(
            P(None, None, None, antennas, "tm"),
            P(antennas, None, None, None, None),
            P(),
            P(antennas, None, "tm", None),
            P("tm"),
        ),
        out_specs=P(antennas, None, None, "tm", None),
        check_vma=False,
    )
```

```python
import math

import jax
import jax.numpy as jnp
from jax import lax
from jax.sharding import PartitionSpec as P


def mixing_matrix(weight_rows, axis):
    real_part = lax.index_in_dim(weight_rows, 0, axis, keepdims=False)
    imag_part = lax.index_in_dim(weight_rows, 1, axis, keepdims=False)
    upper = jnp.stack([real_part, -imag_part], axis=-2)
    lower = jnp.stack([imag_part, real_part], axis=-2)
    return jnp.stack([upper, lower], axis=axis)


def fourier_tables(extent):
    counter = jnp.arange(extent, dtype=jnp.int32)
    phase = counter[:, None] * counter[None, :] % extent
    angle = phase.astype(jnp.float32) * (2.0 * math.pi / extent)
    return lax.optimization_barrier((jnp.cos(angle), jnp.sin(angle)))


def product(left, right):
    return jnp.matmul(left, right, precision=lax.Precision.HIGH)


def build_dedispersion(sweep_response_taps, chirp_length):
    longest = sweep_response_taps.shape[3]
    block_size = 2 * longest
    cosines, sines = fourier_tables(block_size)
    lag = jnp.arange(longest, dtype=jnp.int32)
    inside = lag[None, :] < chirp_length[:, None]
    factor = lax.rsqrt(chirp_length.astype(jnp.float32))[:, None]
    resp_real = jnp.where(inside, sweep_response_taps[0, 0], 0.0) * factor
    resp_imag = jnp.where(inside, sweep_response_taps[0, 1], 0.0) * factor
    freq_real = product(resp_real, cosines[:longest]) + product(resp_imag, sines[:longest])
    freq_imag = product(resp_imag, cosines[:longest]) - product(resp_real, sines[:longest])
    gain_real = freq_real[:, None, :]
    gain_imag = freq_imag[:, None, :]
    back_cos = cosines[:, longest:]
    back_sin = sines[:, longest:]

    def dedisperse(series):
        total = series.shape[3]
        count = total // longest
        padding = jnp.zeros(series.shape[:3] + (longest,), jnp.float32)
        padded = jnp.concatenate([padding, series], axis=3)
        front = padded[..., :total].reshape(series.shape[:3] + (count, longest))
        behind = padded[..., longest:].reshape(series.shape[:3] + (count, longest))
        blocks = jnp.concatenate([front, behind], axis=4)
        spec_real = product(blocks[0], cosines) + product(blocks[1], sines)
        spec_imag = product(blocks[1], cosines) - product(blocks[0], sines)
        prod_real = spec_real * gain_real - spec_imag * gain_imag
        prod_imag = spec_real * gain_imag + spec_imag * gain_real
        out_real = (product(prod_real, back_cos) - product(prod_imag, back_sin)) / block_size
        out_imag = (product(prod_imag, back_cos) + product(prod_real, back_sin)) / block_size
        return jnp.stack([out_real, out_imag], 0).reshape(series.shape)

    return dedisperse


def ring_reduce_scatter(chunks, axis, size, split_axis):
    position = lax.axis_index(axis)
    halves = jnp.split(chunks, 2, axis=split_axis)
    forward = [(i, (i + 1) % size) for i in range(size)]
    backward = [(i, (i - 1) % size) for i in range(size)]

    def pick(part, index):
        return lax.dynamic_index_in_dim(part, index % size, 0, keepdims=False)

    acc_cw = pick(halves[0], position - 1)
    acc_ccw = pick(halves[1], position + 1)
    for step in range(size - 1):
        acc_cw = lax.ppermute(acc_cw, axis, forward) + pick(halves[0], position - step - 2)
        acc_ccw = lax.ppermute(acc_ccw, axis, backward) + pick(halves[1], position + step + 2)
    return jnp.concatenate([acc_cw, acc_ccw], axis=split_axis - 1)


def on_device(voltages, weights, channel_map, sweep_response_taps, chirp_length):
    zs, xs, cs = lax.axis_size("z"), lax.axis_size("x"), lax.axis_size("c")
    order = channel_map.reshape(zs, xs, cs).transpose(2, 0, 1)
    selected = jnp.moveaxis(jnp.take(voltages, order, axis=2, mode="clip"), 2, 0)
    own = lax.all_to_all(selected, "c", split_axis=0, concat_axis=5, tiled=True)[0]
    local_weights = lax.all_to_all(weights, ("z", "x"), split_axis=4, concat_axis=0, tiled=True)
    local_weights = local_weights.reshape((zs, xs) + local_weights.shape[1:])
    mixing = mixing_matrix(local_weights, 2)
    partial = jnp.einsum(
        "zxopbra,rpzxat->zxopbt",
        mixing,
        own,
        preferred_element_type=jnp.float32,
    )
    partial = ring_reduce_scatter(partial, "z", zs, 2)
    beams = ring_reduce_scatter(partial, "x", xs, 1)
    dedisperse = build_dedispersion(sweep_response_taps, chirp_length)
    result = dedisperse(lax.all_to_all(beams, "tm", split_axis=2, concat_axis=3, tiled=True))
    return result[None]


def solution(mesh):
    chan = mesh.shape["chan"]
    zs = 8 if chan % 8 == 0 and chan >= 16 else 1
    grid = mesh.devices.reshape(zs, chan // zs // 2, 2, mesh.shape["tm"])
    fine = jax.sharding.Mesh(grid, ("z", "x", "c", "tm"))
    antennas = ("z", "x", "c")
    return jax.shard_map(
        on_device,
        mesh=fine,
        in_specs=(
            P(None, None, None, antennas, "tm"),
            P(antennas, None, None, None, None),
            P(),
            P(antennas, None, "tm", None),
            P("tm"),
        ),
        out_specs=P(antennas, None, None, "tm", None),
        check_vma=False,
    )
```

```python
import math

import jax
import jax.numpy as jnp
from jax import lax
from jax.sharding import PartitionSpec as P


def mixing_matrix(weight_rows, axis):
    real_part = lax.index_in_dim(weight_rows, 0, axis, keepdims=False)
    imag_part = lax.index_in_dim(weight_rows, 1, axis, keepdims=False)
    upper = jnp.stack([real_part, -imag_part], axis=-2)
    lower = jnp.stack([imag_part, real_part], axis=-2)
    return jnp.stack([upper, lower], axis=axis)


def fourier_tables(extent):
    counter = jnp.arange(extent, dtype=jnp.int32)
    phase = counter[:, None] * counter[None, :] % extent
    angle = phase.astype(jnp.float32) * (2.0 * math.pi / extent)
    return lax.optimization_barrier((jnp.cos(angle), jnp.sin(angle)))


def product(left, right):
    return jnp.matmul(left, right, precision=lax.Precision.HIGH)


def build_dedispersion(sweep_response_taps, chirp_length):
    longest = sweep_response_taps.shape[3]
    block_size = 2 * longest
    cosines, sines = fourier_tables(block_size)
    lag = jnp.arange(longest, dtype=jnp.int32)
    inside = lag[None, :] < chirp_length[:, None]
    factor = lax.rsqrt(chirp_length.astype(jnp.float32))[:, None]
    resp_real = jnp.where(inside, sweep_response_taps[0, 0], 0.0) * factor
    resp_imag = jnp.where(inside, sweep_response_taps[0, 1], 0.0) * factor
    freq_real = product(resp_real, cosines[:longest]) + product(resp_imag, sines[:longest])
    freq_imag = product(resp_imag, cosines[:longest]) - product(resp_real, sines[:longest])
    gain_real = freq_real[:, None, :]
    gain_imag = freq_imag[:, None, :]
    back_cos = cosines[:, longest:]
    back_sin = sines[:, longest:]

    def dedisperse(series):
        total = series.shape[3]
        count = total // longest
        padding = jnp.zeros(series.shape[:3] + (longest,), jnp.float32)
        padded = jnp.concatenate([padding, series], axis=3)
        front = padded[..., :total].reshape(series.shape[:3] + (count, longest))
        behind = padded[..., longest:].reshape(series.shape[:3] + (count, longest))
        blocks = jnp.concatenate([front, behind], axis=4)
        spec_real = product(blocks[0], cosines) + product(blocks[1], sines)
        spec_imag = product(blocks[1], cosines) - product(blocks[0], sines)
        prod_real = spec_real * gain_real - spec_imag * gain_imag
        prod_imag = spec_real * gain_imag + spec_imag * gain_real
        out_real = (product(prod_real, back_cos) - product(prod_imag, back_sin)) / block_size
        out_imag = (product(prod_imag, back_cos) + product(prod_real, back_sin)) / block_size
        return jnp.stack([out_real, out_imag], 0).reshape(series.shape)

    return dedisperse


def ring_reduce_scatter(chunks, axis, size, split_axis):
    position = lax.axis_index(axis)
    half = chunks.shape[split_axis] // 2
    forward = [(i, (i + 1) % size) for i in range(size)]
    backward = [(i, (i - 1) % size) for i in range(size)]

    def pick(which, index):
        chunk = lax.dynamic_index_in_dim(chunks, index % size, 0, keepdims=False)
        return lax.slice_in_dim(chunk, which * half, (which + 1) * half, axis=split_axis - 1)

    acc_cw = pick(0, position - 1)
    acc_ccw = pick(1, position + 1)
    for step in range(size - 1):
        acc_cw = lax.ppermute(acc_cw, axis, forward) + pick(0, position - step - 2)
        acc_ccw = lax.ppermute(acc_ccw, axis, backward) + pick(1, position + step + 2)
    return jnp.concatenate([acc_cw, acc_ccw], axis=split_axis - 1)


def on_device(voltages, weights, channel_map, sweep_response_taps, chirp_length):
    zs, xs, cs = lax.axis_size("z"), lax.axis_size("x"), lax.axis_size("c")
    order = channel_map.reshape(zs, xs, cs).transpose(2, 0, 1)
    selected = jnp.moveaxis(jnp.take(voltages, order, axis=2, mode="clip"), 2, 0)
    own = lax.all_to_all(selected, "c", split_axis=0, concat_axis=5, tiled=True)[0]
    local_weights = lax.all_to_all(weights, ("z", "x"), split_axis=4, concat_axis=0, tiled=True)
    local_weights = local_weights.reshape((zs, xs) + local_weights.shape[1:])
    mixing = mixing_matrix(local_weights, 2)
    partial = jnp.einsum(
        "zxopbra,rpzxat->zxopbt",
        mixing,
        own,
        preferred_element_type=jnp.float32,
    )
    partial = ring_reduce_scatter(partial, "z", zs, 2)
    beams = ring_reduce_scatter(partial, "x", xs, 1)
    dedisperse = build_dedispersion(sweep_response_taps, chirp_length)
    result = dedisperse(lax.all_to_all(beams, "tm", split_axis=2, concat_axis=3, tiled=True))
    return result[None]


def solution(mesh):
    chan = mesh.shape["chan"]
    zs = 8 if chan % 8 == 0 and chan >= 16 else 1
    grid = mesh.devices.reshape(zs, chan // zs // 2, 2, mesh.shape["tm"])
    fine = jax.sharding.Mesh(grid, ("z", "x", "c", "tm"))
    antennas = ("z", "x", "c")
    return jax.shard_map(
        on_device,
        mesh=fine,
        in_specs=(
            P(None, None, None, antennas, "tm"),
            P(antennas, None, None, None, None),
            P(),
            P(antennas, None, "tm", None),
            P("tm"),
        ),
        out_specs=P(antennas, None, None, "tm", None),
        check_vma=False,
    )
```

```python
import math

import jax
import jax.numpy as jnp
from jax import lax
from jax.sharding import PartitionSpec as P


def mixing_matrix(weight_rows, axis):
    real_part = lax.index_in_dim(weight_rows, 0, axis, keepdims=False)
    imag_part = lax.index_in_dim(weight_rows, 1, axis, keepdims=False)
    upper = jnp.stack([real_part, -imag_part], axis=-2)
    lower = jnp.stack([imag_part, real_part], axis=-2)
    return jnp.stack([upper, lower], axis=axis)


def fourier_tables(extent):
    counter = jnp.arange(extent, dtype=jnp.int32)
    phase = counter[:, None] * counter[None, :] % extent
    angle = phase.astype(jnp.float32) * (2.0 * math.pi / extent)
    return lax.optimization_barrier((jnp.cos(angle), jnp.sin(angle)))


def product(left, right):
    return jnp.matmul(left, right, precision=lax.Precision.HIGH)


def build_dedispersion(sweep_response_taps, chirp_length):
    longest = sweep_response_taps.shape[3]
    block_size = 2 * longest
    cosines, sines = fourier_tables(block_size)
    lag = jnp.arange(longest, dtype=jnp.int32)
    inside = lag[None, :] < chirp_length[:, None]
    factor = lax.rsqrt(chirp_length.astype(jnp.float32))[:, None]
    resp_real = jnp.where(inside, sweep_response_taps[0, 0], 0.0) * factor
    resp_imag = jnp.where(inside, sweep_response_taps[0, 1], 0.0) * factor
    freq_real = product(resp_real, cosines[:longest]) + product(resp_imag, sines[:longest])
    freq_imag = product(resp_imag, cosines[:longest]) - product(resp_real, sines[:longest])
    gain_real = freq_real[:, None, :]
    gain_imag = freq_imag[:, None, :]
    back_cos = cosines[:, longest:]
    back_sin = sines[:, longest:]

    def dedisperse(series):
        total = series.shape[3]
        count = total // longest
        padding = jnp.zeros(series.shape[:3] + (longest,), jnp.float32)
        padded = jnp.concatenate([padding, series], axis=3)
        front = padded[..., :total].reshape(series.shape[:3] + (count, longest))
        behind = padded[..., longest:].reshape(series.shape[:3] + (count, longest))
        blocks = jnp.concatenate([front, behind], axis=4)
        spec_real = product(blocks[0], cosines) + product(blocks[1], sines)
        spec_imag = product(blocks[1], cosines) - product(blocks[0], sines)
        prod_real = spec_real * gain_real - spec_imag * gain_imag
        prod_imag = spec_real * gain_imag + spec_imag * gain_real
        out_real = (product(prod_real, back_cos) - product(prod_imag, back_sin)) / block_size
        out_imag = (product(prod_imag, back_cos) + product(prod_real, back_sin)) / block_size
        return jnp.stack([out_real, out_imag], 0).reshape(series.shape)

    return dedisperse


def ring_reduce_scatter(halves, axis, size):
    position = lax.axis_index(axis)
    forward = [(i, (i + 1) % size) for i in range(size)]
    backward = [(i, (i - 1) % size) for i in range(size)]

    def pick(part, index):
        return lax.dynamic_index_in_dim(part, index % size, 0, keepdims=False)

    acc_cw = pick(halves[0], position - 1)
    acc_ccw = pick(halves[1], position + 1)
    for step in range(size - 1):
        acc_cw = lax.ppermute(acc_cw, axis, forward) + pick(halves[0], position - step - 2)
        acc_ccw = lax.ppermute(acc_ccw, axis, backward) + pick(halves[1], position + step + 2)
    return acc_cw, acc_ccw


def on_device(voltages, weights, channel_map, sweep_response_taps, chirp_length):
    zs, xs, cs = lax.axis_size("z"), lax.axis_size("x"), lax.axis_size("c")
    order = channel_map.reshape(zs, xs, cs).transpose(2, 0, 1)
    selected = jnp.moveaxis(jnp.take(voltages, order, axis=2, mode="clip"), 2, 0)
    own = lax.all_to_all(selected, "c", split_axis=0, concat_axis=5, tiled=True)[0]
    local_weights = lax.all_to_all(weights, ("z", "x"), split_axis=4, concat_axis=0, tiled=True)
    local_weights = local_weights.reshape((zs, xs) + local_weights.shape[1:])
    mixing = mixing_matrix(local_weights, 2)
    parts = [
        jnp.einsum(
            "zxpbra,rpzxat->zxpbt", mixing[:, :, o], own, preferred_element_type=jnp.float32
        )
        for o in range(2)
    ]
    parts = ring_reduce_scatter(parts, "z", zs)
    parts = ring_reduce_scatter(parts, "x", xs)
    beams = jnp.stack(parts, axis=0)
    dedisperse = build_dedispersion(sweep_response_taps, chirp_length)
    result = dedisperse(lax.all_to_all(beams, "tm", split_axis=2, concat_axis=3, tiled=True))
    return result[None]


def solution(mesh):
    chan = mesh.shape["chan"]
    zs = 8 if chan % 8 == 0 and chan >= 16 else 1
    grid = mesh.devices.reshape(zs, chan // zs // 2, 2, mesh.shape["tm"])
    fine = jax.sharding.Mesh(grid, ("z", "x", "c", "tm"))
    antennas = ("z", "x", "c")
    return jax.shard_map(
        on_device,
        mesh=fine,
        in_specs=(
            P(None, None, None, antennas, "tm"),
            P(antennas, None, None, None, None),
            P(),
            P(antennas, None, "tm", None),
            P("tm"),
        ),
        out_specs=P(antennas, None, None, "tm", None),
        check_vma=False,
    )
```

```python
import math

import jax
import jax.numpy as jnp
from jax import lax
from jax.sharding import PartitionSpec as P


def mixing_matrix(weight_rows, axis):
    real_part = lax.index_in_dim(weight_rows, 0, axis, keepdims=False)
    imag_part = lax.index_in_dim(weight_rows, 1, axis, keepdims=False)
    upper = jnp.stack([real_part, -imag_part], axis=-2)
    lower = jnp.stack([imag_part, real_part], axis=-2)
    return jnp.stack([upper, lower], axis=axis)


def fourier_tables(extent):
    counter = jnp.arange(extent, dtype=jnp.int32)
    phase = counter[:, None] * counter[None, :] % extent
    angle = phase.astype(jnp.float32) * (2.0 * math.pi / extent)
    return lax.optimization_barrier((jnp.cos(angle), jnp.sin(angle)))


def product(left, right):
    return jnp.matmul(left, right, precision=lax.Precision.HIGH)


def build_dedispersion(sweep_response_taps, chirp_length):
    longest = sweep_response_taps.shape[3]
    block_size = 2 * longest
    cosines, sines = fourier_tables(block_size)
    lag = jnp.arange(longest, dtype=jnp.int32)
    inside = lag[None, :] < chirp_length[:, None]
    factor = lax.rsqrt(chirp_length.astype(jnp.float32))[:, None]
    resp_real = jnp.where(inside, sweep_response_taps[0, 0], 0.0) * factor
    resp_imag = jnp.where(inside, sweep_response_taps[0, 1], 0.0) * factor
    freq_real = product(resp_real, cosines[:longest]) + product(resp_imag, sines[:longest])
    freq_imag = product(resp_imag, cosines[:longest]) - product(resp_real, sines[:longest])
    gain_real = freq_real[:, None, :]
    gain_imag = freq_imag[:, None, :]
    back_cos = cosines[:, longest:]
    back_sin = sines[:, longest:]

    def dedisperse(series):
        total = series.shape[3]
        count = total // longest
        padding = jnp.zeros(series.shape[:3] + (longest,), jnp.float32)
        padded = jnp.concatenate([padding, series], axis=3)
        front = padded[..., :total].reshape(series.shape[:3] + (count, longest))
        behind = padded[..., longest:].reshape(series.shape[:3] + (count, longest))
        blocks = jnp.concatenate([front, behind], axis=4)
        spec_real = product(blocks[0], cosines) + product(blocks[1], sines)
        spec_imag = product(blocks[1], cosines) - product(blocks[0], sines)
        prod_real = spec_real * gain_real - spec_imag * gain_imag
        prod_imag = spec_real * gain_imag + spec_imag * gain_real
        out_real = (product(prod_real, back_cos) - product(prod_imag, back_sin)) / block_size
        out_imag = (product(prod_imag, back_cos) + product(prod_real, back_sin)) / block_size
        return jnp.stack([out_real, out_imag], 0).reshape(series.shape)

    return dedisperse


def ring_reduce_scatter(halves, axis, size):
    position = lax.axis_index(axis)
    forward = [(i, (i + 1) % size) for i in range(size)]
    backward = [(i, (i - 1) % size) for i in range(size)]

    def pick(part, index):
        return lax.dynamic_index_in_dim(part, index % size, 0, keepdims=False)

    acc_cw = pick(halves[0], position - 1)
    acc_ccw = pick(halves[1], position + 1)
    for step in range(size - 1):
        acc_cw = lax.ppermute(acc_cw, axis, forward) + pick(halves[0], position - step - 2)
        acc_ccw = lax.ppermute(acc_ccw, axis, backward) + pick(halves[1], position + step + 2)
    return acc_cw, acc_ccw


def on_device(voltages, weights, channel_map, sweep_response_taps, chirp_length):
    zs, xs, cs = lax.axis_size("z"), lax.axis_size("x"), lax.axis_size("c")
    order = channel_map.reshape(zs, xs, cs).transpose(2, 0, 1)
    selected = jnp.moveaxis(jnp.take(voltages, order, axis=2, mode="clip"), 2, 0)
    own = lax.all_to_all(selected, "c", split_axis=0, concat_axis=5, tiled=True)[0]
    groups = zs * xs
    grouped = weights[0].reshape(weights.shape[1:4] + (groups, -1))
    grouped = jnp.moveaxis(grouped, 3, 0)
    local_weights = lax.all_to_all(grouped, ("z", "x"), split_axis=0, concat_axis=0, tiled=True)
    local_weights = local_weights.reshape((zs, xs) + local_weights.shape[1:])
    mixing = mixing_matrix(local_weights, 2)
    parts = [
        jnp.einsum(
            "zxpbra,rpzxat->zxpbt", mixing[:, :, o], own, preferred_element_type=jnp.float32
        )
        for o in range(2)
    ]
    parts = ring_reduce_scatter(parts, "z", zs)
    parts = ring_reduce_scatter(parts, "x", xs)
    beams = jnp.stack(parts, axis=0)
    dedisperse = build_dedispersion(sweep_response_taps, chirp_length)
    result = dedisperse(lax.all_to_all(beams, "tm", split_axis=2, concat_axis=3, tiled=True))
    return result[None]


def solution(mesh):
    chan = mesh.shape["chan"]
    zs = 8 if chan % 8 == 0 and chan >= 16 else 1
    grid = mesh.devices.reshape(zs, chan // zs // 2, 2, mesh.shape["tm"])
    fine = jax.sharding.Mesh(grid, ("z", "x", "c", "tm"))
    antennas = ("z", "x", "c")
    return jax.shard_map(
        on_device,
        mesh=fine,
        in_specs=(
            P(None, None, None, antennas, "tm"),
            P(antennas, None, None, None, None),
            P(),
            P(antennas, None, "tm", None),
            P("tm"),
        ),
        out_specs=P(antennas, None, None, "tm", None),
        check_vma=False,
    )
```

```python
import math

import jax
import jax.numpy as jnp
from jax import lax
from jax.sharding import PartitionSpec as P


def mixing_matrix(weight_rows, axis):
    real_part = lax.index_in_dim(weight_rows, 0, axis, keepdims=False)
    imag_part = lax.index_in_dim(weight_rows, 1, axis, keepdims=False)
    upper = jnp.stack([real_part, -imag_part], axis=-2)
    lower = jnp.stack([imag_part, real_part], axis=-2)
    return jnp.stack([upper, lower], axis=axis)


def fourier_tables(extent):
    counter = jnp.arange(extent, dtype=jnp.int32)
    phase = counter[:, None] * counter[None, :] % extent
    angle = phase.astype(jnp.float32) * (2.0 * math.pi / extent)
    return lax.optimization_barrier((jnp.cos(angle), jnp.sin(angle)))


def product(left, right):
    return jnp.matmul(left, right, precision=lax.Precision.HIGH)


def build_dedispersion(sweep_response_taps, chirp_length):
    longest = sweep_response_taps.shape[3]
    block_size = 2 * longest
    cosines, sines = fourier_tables(block_size)
    lag = jnp.arange(longest, dtype=jnp.int32)
    inside = lag[None, :] < chirp_length[:, None]
    factor = lax.rsqrt(chirp_length.astype(jnp.float32))[:, None]
    resp_real = jnp.where(inside, sweep_response_taps[0, 0], 0.0) * factor
    resp_imag = jnp.where(inside, sweep_response_taps[0, 1], 0.0) * factor
    freq_real = product(resp_real, cosines[:longest]) + product(resp_imag, sines[:longest])
    freq_imag = product(resp_imag, cosines[:longest]) - product(resp_real, sines[:longest])
    gain_real = freq_real[:, None, :]
    gain_imag = freq_imag[:, None, :]
    back_cos = cosines[:, longest:]
    back_sin = sines[:, longest:]

    def dedisperse(series):
        total = series.shape[3]
        count = total // longest
        padding = jnp.zeros(series.shape[:3] + (longest,), jnp.float32)
        padded = jnp.concatenate([padding, series], axis=3)
        front = padded[..., :total].reshape(series.shape[:3] + (count, longest))
        behind = padded[..., longest:].reshape(series.shape[:3] + (count, longest))
        blocks = jnp.concatenate([front, behind], axis=4)
        spec_real = product(blocks[0], cosines) + product(blocks[1], sines)
        spec_imag = product(blocks[1], cosines) - product(blocks[0], sines)
        prod_real = spec_real * gain_real - spec_imag * gain_imag
        prod_imag = spec_real * gain_imag + spec_imag * gain_real
        out_real = (product(prod_real, back_cos) - product(prod_imag, back_sin)) / block_size
        out_imag = (product(prod_imag, back_cos) + product(prod_real, back_sin)) / block_size
        return jnp.stack([out_real, out_imag], 0).reshape(series.shape)

    return dedisperse


def ring_reduce_scatter(halves, axis, size):
    position = lax.axis_index(axis)
    forward = [(i, (i + 1) % size) for i in range(size)]
    backward = [(i, (i - 1) % size) for i in range(size)]

    def pick(part, index):
        return lax.dynamic_index_in_dim(part, index % size, 0, keepdims=False)

    acc_cw = pick(halves[0], position - 1)
    acc_ccw = pick(halves[1], position + 1)
    for step in range(size - 1):
        acc_cw = lax.ppermute(acc_cw, axis, forward) + pick(halves[0], position - step - 2)
        acc_ccw = lax.ppermute(acc_ccw, axis, backward) + pick(halves[1], position + step + 2)
    return acc_cw, acc_ccw


def on_device(voltages, weights, channel_map, sweep_response_taps, chirp_length):
    zs, xs, cs = lax.axis_size("z"), lax.axis_size("x"), lax.axis_size("c")
    order = channel_map.reshape(zs, xs, cs).transpose(2, 0, 1)
    selected = jnp.moveaxis(jnp.take(voltages, order, axis=2, mode="clip"), 2, 0)
    groups = zs * xs
    grouped = weights[0].reshape(weights.shape[1:4] + (groups, -1))
    grouped = jnp.moveaxis(grouped, 3, 0)
    local_weights = lax.all_to_all(grouped, ("z", "x"), split_axis=0, concat_axis=0, tiled=True)
    selected = selected + local_weights[0, 0, 0, 0, 0] * 0
    own = lax.all_to_all(selected, "c", split_axis=0, concat_axis=5, tiled=True)[0]
    local_weights = local_weights.reshape((zs, xs) + local_weights.shape[1:])
    mixing = mixing_matrix(local_weights, 2)
    parts = [
        jnp.einsum(
            "zxpbra,rpzxat->zxpbt", mixing[:, :, o], own, preferred_element_type=jnp.float32
        )
        for o in range(2)
    ]
    parts = ring_reduce_scatter(parts, "z", zs)
    parts = ring_reduce_scatter(parts, "x", xs)
    beams = jnp.stack(parts, axis=0)
    dedisperse = build_dedispersion(sweep_response_taps, chirp_length)
    result = dedisperse(lax.all_to_all(beams, "tm", split_axis=2, concat_axis=3, tiled=True))
    return result[None]


def solution(mesh):
    chan = mesh.shape["chan"]
    zs = 8 if chan % 8 == 0 and chan >= 16 else 1
    grid = mesh.devices.reshape(zs, chan // zs // 2, 2, mesh.shape["tm"])
    fine = jax.sharding.Mesh(grid, ("z", "x", "c", "tm"))
    antennas = ("z", "x", "c")
    return jax.shard_map(
        on_device,
        mesh=fine,
        in_specs=(
            P(None, None, None, antennas, "tm"),
            P(antennas, None, None, None, None),
            P(),
            P(antennas, None, "tm", None),
            P("tm"),
        ),
        out_specs=P(antennas, None, None, "tm", None),
        check_vma=False,
    )
```

```python
import math

import jax
import jax.numpy as jnp
from jax import lax
from jax.sharding import PartitionSpec as P


def mixing_matrix(weight_rows, axis):
    real_part = lax.index_in_dim(weight_rows, 0, axis, keepdims=False)
    imag_part = lax.index_in_dim(weight_rows, 1, axis, keepdims=False)
    upper = jnp.stack([real_part, -imag_part], axis=-2)
    lower = jnp.stack([imag_part, real_part], axis=-2)
    return jnp.stack([upper, lower], axis=axis)


def fourier_tables(extent):
    counter = jnp.arange(extent, dtype=jnp.int32)
    phase = counter[:, None] * counter[None, :] % extent
    angle = phase.astype(jnp.float32) * (2.0 * math.pi / extent)
    return lax.optimization_barrier((jnp.cos(angle), jnp.sin(angle)))


def product(left, right):
    return jnp.matmul(left, right, precision=lax.Precision.HIGH)


def build_dedispersion(sweep_response_taps, chirp_length):
    longest = sweep_response_taps.shape[3]
    block_size = 2 * longest
    cosines, sines = fourier_tables(block_size)
    lag = jnp.arange(longest, dtype=jnp.int32)
    inside = lag[None, :] < chirp_length[:, None]
    factor = lax.rsqrt(chirp_length.astype(jnp.float32))[:, None]
    resp_real = jnp.where(inside, sweep_response_taps[0, 0], 0.0) * factor
    resp_imag = jnp.where(inside, sweep_response_taps[0, 1], 0.0) * factor
    freq_real = product(resp_real, cosines[:longest]) + product(resp_imag, sines[:longest])
    freq_imag = product(resp_imag, cosines[:longest]) - product(resp_real, sines[:longest])
    gain_real = freq_real[:, None, :]
    gain_imag = freq_imag[:, None, :]
    back_cos = cosines[:, longest:]
    back_sin = sines[:, longest:]

    def dedisperse(series):
        total = series.shape[3]
        count = total // longest
        padding = jnp.zeros(series.shape[:3] + (longest,), jnp.float32)
        padded = jnp.concatenate([padding, series], axis=3)
        front = padded[..., :total].reshape(series.shape[:3] + (count, longest))
        behind = padded[..., longest:].reshape(series.shape[:3] + (count, longest))
        blocks = jnp.concatenate([front, behind], axis=4)
        spec_real = product(blocks[0], cosines) + product(blocks[1], sines)
        spec_imag = product(blocks[1], cosines) - product(blocks[0], sines)
        prod_real = spec_real * gain_real - spec_imag * gain_imag
        prod_imag = spec_real * gain_imag + spec_imag * gain_real
        out_real = (product(prod_real, back_cos) - product(prod_imag, back_sin)) / block_size
        out_imag = (product(prod_imag, back_cos) + product(prod_real, back_sin)) / block_size
        return jnp.stack([out_real, out_imag], 0).reshape(series.shape)

    return dedisperse


def ring_reduce_scatter(halves, axis, size):
    position = lax.axis_index(axis)
    forward = [(i, (i + 1) % size) for i in range(size)]
    backward = [(i, (i - 1) % size) for i in range(size)]

    def pick(part, index):
        return lax.dynamic_index_in_dim(part, index % size, 0, keepdims=False)

    acc_cw = pick(halves[0], position - 1)
    acc_ccw = pick(halves[1], position + 1)
    for step in range(size - 1):
        acc_cw = lax.ppermute(acc_cw, axis, forward) + pick(halves[0], position - step - 2)
        acc_ccw = lax.ppermute(acc_ccw, axis, backward) + pick(halves[1], position + step + 2)
    return acc_cw, acc_ccw


def on_device(voltages, weights, channel_map, sweep_response_taps, chirp_length):
    zs, xs, cs = lax.axis_size("z"), lax.axis_size("x"), lax.axis_size("c")
    order = channel_map.reshape(zs, xs, cs).transpose(2, 0, 1)
    selected = jnp.moveaxis(jnp.take(voltages, order, axis=2, mode="clip"), 2, 0)
    own = lax.all_to_all(selected, "c", split_axis=0, concat_axis=5, tiled=True)[0]
    groups = zs * xs
    grouped = weights[0].reshape(weights.shape[1:4] + (groups, -1))
    grouped = jnp.moveaxis(grouped, 3, 0)
    local_weights = lax.all_to_all(grouped, ("z", "x"), split_axis=0, concat_axis=0, tiled=True)
    local_weights = local_weights.reshape((zs, xs) + local_weights.shape[1:])
    mixing = mixing_matrix(local_weights, 2)
    both = jnp.einsum("zxopbra,rpzxat->ozxpbt", mixing, own, preferred_element_type=jnp.float32)
    parts = [both[0], both[1]]
    parts = ring_reduce_scatter(parts, "z", zs)
    parts = ring_reduce_scatter(parts, "x", xs)
    beams = jnp.stack(parts, axis=0)
    dedisperse = build_dedispersion(sweep_response_taps, chirp_length)
    result = dedisperse(lax.all_to_all(beams, "tm", split_axis=2, concat_axis=3, tiled=True))
    return result[None]


def solution(mesh):
    chan = mesh.shape["chan"]
    zs = 8 if chan % 8 == 0 and chan >= 16 else 1
    grid = mesh.devices.reshape(zs, chan // zs // 2, 2, mesh.shape["tm"])
    fine = jax.sharding.Mesh(grid, ("z", "x", "c", "tm"))
    antennas = ("z", "x", "c")
    return jax.shard_map(
        on_device,
        mesh=fine,
        in_specs=(
            P(None, None, None, antennas, "tm"),
            P(antennas, None, None, None, None),
            P(),
            P(antennas, None, "tm", None),
            P("tm"),
        ),
        out_specs=P(antennas, None, None, "tm", None),
        check_vma=False,
    )
```
